512 devices in a mesh: tau: 8 (over x, core), blk: 64 (over z, y).
Axes of the slice: x: 4, y: 8, z: 8, core: 2. Of those that a mesh axis runs over, the one named last changes fastest.
Arguments:
- three_center: bfloat16 [64, 128, 128, 128], P('blk'), may hold values from -0.59765625 to 0.59765625
- green_blocks: bfloat16 [8, 512, 2048], P('tau', 'blk'), may hold values from -0.5 to 0.5
- block_owner: int32 [3072], P('blk'), may hold values from 0 to 63, as said below
- block_slot: int32 [3072], P('blk'), may hold values from 0 to 7
- fold_weights: float32 [8, 8], P(None, 'tau'), may hold values from -1 to 1
Outputs:
- chi_freq: float32 [8, 8192, 384], P('tau', 'blk')
The draws below stay inside these ranges and needn't reach their ends.
Inputs may be any that keep to these rules, and one draw needn't show every extreme that they name: `block_owner`: among the 48 entries of each auxiliary block, no owner appears more than 2 times, and one owner appears exactly 2 times in the entries of every auxiliary block.
All inputs are finite; a program needn't handle non-finite values.
Results may differ from the reference program's by a relative error of at most 0.0041.
Values may be sent and summed in bfloat16 or wider, within the bound.
No kernel may reach another device: no remote copies, remote signals or barrier semaphores. Data moves between devices by JAX's collectives and lax.ppermute only.
A program may use at most 128 MiB of HBM per device.

```python
import jax
import jax.numpy as jnp
from jax import lax

AB = 32
NS = 4
AUXB = 128
HALF = 1
G_DEV = 8
RW = 128
NPART = 3
NREQ = 48
NAUXB = 64
NAUX = 8192
NTAU = 8
NFREQ = 8
GBLOCKS = 512
CAP = 2


def draw_block_owner(key, part):
    busiest = jax.random.randint(jax.random.fold_in(key, 7919), (), 0, NAUXB).astype(jnp.int32)

    def device_owners(device_index):
        device_key = jax.random.fold_in(key, device_index)
        others = jax.random.permutation(jax.random.fold_in(device_key, 1), NAUXB - 1).astype(jnp.int32)
        row_index = jnp.arange(NREQ - CAP, dtype=jnp.int32)
        other_owner = others[row_index % (NAUXB - 1)]
        other_owner = other_owner + (other_owner >= busiest).astype(jnp.int32)
        assigned = jnp.concatenate([jnp.full((CAP,), busiest, dtype=jnp.int32), other_owner])
        shuffle = jax.random.permutation(jax.random.fold_in(device_key, 2), NREQ)
        return assigned[shuffle]
    owners = jax.vmap(device_owners)(jnp.arange(NAUXB, dtype=jnp.int32))
    return owners.reshape(-1).astype(jnp.int32)


def touch_ends(drawn, stream_key, smallest, top_value):
    extent = drawn.shape
    place = [jax.random.randint(jax.random.fold_in(stream_key, axis), (), 0, extent[axis]) for axis in range(len(extent))]
    drawn = drawn.at[tuple(place)].set(smallest)
    longest = extent.index(max(extent))
    place[longest] = (place[longest] + 1) % extent[longest]
    return drawn.at[tuple(place)].set(top_value)


def steps_of(own_key, dims, cuts, smallest, largest):
    loudness = 1.0
    for axis_at, blocks in cuts:
        draws = jax.random.uniform(jax.random.fold_in(jax.random.fold_in(own_key, 6), axis_at), (blocks,), jnp.float32, smallest / len(cuts), largest / len(cuts))
        loudness = loudness * jnp.repeat(jnp.exp(draws), dims[axis_at] // blocks).reshape((-1,) + (1,) * (len(dims) - 1 - axis_at))
    return loudness


def normal_values(stream_key, dims, width, bound, shards=(), kind=jnp.bfloat16):
    loudness = steps_of(stream_key, dims, shards, -0.22, 0.18) if shards else 1.0
    entries = jax.random.normal(stream_key, dims, jnp.float32) * width * loudness
    return jnp.minimum(jnp.maximum(entries, -bound), bound).astype(kind)


def setup_inputs(seed: int = 0) -> dict:
    keys = jax.random.split(jax.random.key(seed), 6)
    return {
        "three_center": normal_values(keys[0], (NAUXB, RW, RW, AUXB), 0.1, 0.59765625, ((0, 64),)),
        "green_blocks": normal_values(keys[1], (NTAU, GBLOCKS, 2 * AB * AB), RW ** -0.5, 0.5, ((0, 8), (1, 64))),
        "block_owner": draw_block_owner(jax.random.fold_in(keys[5], 71), 0),
        "block_slot": touch_ends(jax.random.randint(keys[3], (NAUXB * NREQ,), 0, G_DEV), jax.random.fold_in(keys[3], 1), 0, G_DEV - 1).astype(jnp.int32),
        "fold_weights": jnp.clip(jax.random.uniform(keys[4], (NFREQ, NTAU), jnp.float32, -1.0, 1.0) * steps_of(keys[4], (NFREQ, NTAU), ((1, 8),), -0.4, 0.0), -1.0, 1.0),
    }


def green_pair(local_table, index_grid):
    blocks = jnp.take(local_table, index_grid.reshape(-1), axis=0)
    blocks = blocks.reshape(NS, NS, 2, AB, AB)
    occupied = blocks[:, :, 0].transpose(0, 2, 1, 3).reshape(NS * AB, NS * AB)
    virtual = blocks[:, :, 1].transpose(0, 2, 1, 3).reshape(NS * AB, NS * AB)
    return occupied, virtual


def transform(occupied, virtual, source):
    region = source.shape[0]
    aux_width = source.shape[2]
    halfway = jnp.einsum("sn,mnb->msb", virtual.astype(jnp.float32), source.astype(jnp.float32)).astype(jnp.bfloat16)
    image_block = jnp.dot(occupied, halfway.reshape(region, region * aux_width), preferred_element_type=jnp.float32)
    return image_block.astype(jnp.bfloat16).reshape(region, region, aux_width)


def pair_block(partner, image_block):
    region = partner.shape[0]
    aux_width = partner.shape[2]
    flat_image = image_block.reshape(region * region, aux_width)
    flat_partner = partner.reshape(region * region, aux_width)
    return -2.0 * jnp.dot(flat_image.T, flat_partner, preferred_element_type=jnp.float32)


def reference(three_center, green_blocks, block_owner, block_slot, fold_weights):
    block_ids = (block_owner * G_DEV + block_slot).astype(jnp.int32).reshape(NAUXB, NPART, NS, NS)

    def column(aux_index):
        source = lax.dynamic_index_in_dim(three_center, aux_index, 0, keepdims=False)
        own_ids = lax.dynamic_index_in_dim(block_ids, aux_index, 0, keepdims=False)
        per_time = []
        for time_index in range(NTAU):
            local_table = green_blocks[time_index]
            pieces = []
            for slot_index in range(NPART):
                occupied, virtual = green_pair(local_table, own_ids[slot_index])
                image_block = transform(occupied, virtual, source)
                partner_index = ((aux_index + slot_index - HALF) % NAUXB).astype(jnp.int32)
                partner = lax.dynamic_index_in_dim(three_center, partner_index, 0, keepdims=False)
                pieces.append(pair_block(partner, image_block))
            per_time.append(jnp.concatenate(pieces, axis=1))
        return jnp.stack(per_time)

    chi_blocks = lax.map(column, jnp.arange(NAUXB, dtype=jnp.int32))
    folded = jnp.einsum("kt,rtbc->krbc", fold_weights, chi_blocks, precision=lax.Precision.HIGHEST)
    return folded.reshape(NFREQ, NAUX, NPART * AUXB)
```

```python
import jax
import jax.numpy as jnp
from jax import lax
from jax.sharding import PartitionSpec as P

AB = 32
NS = 4
HALF = 1


def from_behind(value, axis, by):
    size = lax.axis_size(axis)
    return lax.ppermute(value, axis, [(i, (i + by) % size) for i in range(size)])


def green_pair(blocks):
    blocks = blocks.reshape(NS, NS, 2, AB, AB)
    occupied = blocks[:, :, 0].transpose(0, 2, 1, 3).reshape(NS * AB, NS * AB)
    virtual = blocks[:, :, 1].transpose(0, 2, 1, 3).reshape(NS * AB, NS * AB)
    return (occupied, virtual)


def transform(occupied, virtual, source):
    region = source.shape[0]
    aux_width = source.shape[2]
    halfway = jnp.einsum("sn,mnb->msb", virtual, source, preferred_element_type=jnp.float32).astype(
        jnp.bfloat16
    )
    image_block = jnp.dot(
        occupied, halfway.reshape(region, region * aux_width), preferred_element_type=jnp.float32
    )
    return image_block.astype(jnp.bfloat16).reshape(region, region, aux_width)


def pair_block(partner, image_block):
    region = partner.shape[0]
    aux_width = partner.shape[2]
    flat_image = image_block.reshape(region * region, aux_width)
    flat_partner = partner.reshape(region * region, aux_width)
    product = lax.dot_general(
        flat_image, flat_partner, (((0,), (0,)), ((), ())), preferred_element_type=jnp.float32
    )
    return -2.0 * product


def local(three_center, green_blocks, block_owner, block_slot, fold_weights):
    source = three_center[0]
    local_table = green_blocks[0]
    devices = lax.axis_size("blk")
    requests = block_owner.shape[0]
    per_slot = NS * NS
    capacity = 2 * ((requests + devices - 1) // devices)
    owner_match = (block_owner[:, None] == jnp.arange(devices, dtype=jnp.int32)[None, :]).astype(
        jnp.int32
    )
    position = jnp.sum(jnp.cumsum(owner_match, axis=0) * owner_match, axis=1) - 1
    outgoing = jnp.zeros((devices, capacity), jnp.int32).at[block_owner, position].set(block_slot)
    found_blocks = jnp.take(
        local_table,
        lax.all_to_all(outgoing, "blk", split_axis=0, concat_axis=0, tiled=True),
        axis=0,
    )
    replies = lax.all_to_all(found_blocks, "blk", split_axis=0, concat_axis=0, tiled=True)
    fetched = replies[block_owner, position]
    partners_total = 2 * HALF + 1
    pieces = []
    for slot_index in range(partners_total):
        occupied, virtual = green_pair(fetched[slot_index * per_slot : (slot_index + 1) * per_slot])
        image_block = transform(occupied, virtual, source)
        if slot_index == HALF:
            partner = source
        else:
            partner = from_behind(source, "blk", HALF - slot_index)
        pieces.append(pair_block(partner, image_block))
    chi_time = jnp.concatenate(pieces, axis=1)
    column_weights = fold_weights[:, 0]
    weighted = column_weights[:, None, None] * chi_time[None]
    received = lax.all_to_all(weighted, "tau", split_axis=0, concat_axis=0, tiled=True)
    return jnp.sum(received, axis=0, keepdims=True)


def solution(mesh):
    return jax.shard_map(
        local,
        mesh=mesh,
        in_specs=(
            P("blk", None, None, None),
            P("tau", "blk", None),
            P("blk"),
            P("blk"),
            P(None, "tau"),
        ),
        out_specs=P("tau", "blk", None),
        check_vma=False,
    )
```

```python
import jax
import jax.numpy as jnp
from jax import lax
from jax.sharding import PartitionSpec as P

AB = 32
NS = 4
HALF = 1


def from_behind(value, axis, by):
    size = lax.axis_size(axis)
    return lax.ppermute(value, axis, [(i, (i + by) % size) for i in range(size)])


def green_pair(blocks):
    blocks = blocks.reshape(NS, NS, 2, AB, AB)
    occupied = blocks[:, :, 0].transpose(0, 2, 1, 3).reshape(NS * AB, NS * AB)
    virtual = blocks[:, :, 1].transpose(0, 2, 1, 3).reshape(NS * AB, NS * AB)
    return (occupied, virtual)


def image_of(occupied, virtual, source_t):
    halfway = lax.dot_general(
        source_t, virtual, (((2,), (1,)), ((), ())), preferred_element_type=jnp.float32
    ).astype(jnp.bfloat16)
    image = lax.dot_general(
        halfway, occupied, (((1,), (1,)), ((), ())), preferred_element_type=jnp.float32
    ).astype(jnp.bfloat16)
    return image


def pair_block(partner_t, image):
    aux_width = image.shape[0]
    flat_image = image.reshape(aux_width, -1)
    flat_partner = partner_t.reshape(flat_image.shape[1], -1)
    product = jnp.dot(flat_image, flat_partner, preferred_element_type=jnp.float32)
    return -2.0 * product


def partner_from(own_t, by):
    core = lax.axis_index("tau") % 2
    half = own_t.shape[0] // 2
    mine = lax.dynamic_slice_in_dim(own_t, core * half, half, 0)
    fetched = from_behind(mine, "blk", by)
    size = lax.axis_size("tau")
    other = lax.ppermute(fetched, "tau", [(i, i ^ 1) for i in range(size)])
    low = jnp.where(core == 0, fetched, other)
    high = jnp.where(core == 0, other, fetched)
    return jnp.concatenate([low, high], axis=0)


def local(three_center, green_blocks, block_owner, block_slot, fold_weights):
    source = three_center[0]
    source_t = jnp.transpose(source, (2, 0, 1))
    own_t = jnp.transpose(source, (1, 0, 2))
    partners = [partner_from(own_t, HALF - j) if j != HALF else own_t for j in range(2 * HALF + 1)]
    local_table = green_blocks[0]
    devices = lax.axis_size("blk")
    requests = block_owner.shape[0]
    per_slot = NS * NS
    capacity = 2 * ((requests + devices - 1) // devices)
    owner_match = (block_owner[:, None] == jnp.arange(devices, dtype=jnp.int32)[None, :]).astype(
        jnp.int32
    )
    position = jnp.sum(jnp.cumsum(owner_match, axis=0) * owner_match, axis=1) - 1
    outgoing = jnp.zeros((devices, capacity), jnp.int32).at[block_owner, position].set(block_slot)
    found_blocks = jnp.take(
        local_table,
        lax.all_to_all(outgoing, "blk", split_axis=0, concat_axis=0, tiled=True),
        axis=0,
    )
    replies = lax.all_to_all(found_blocks, "blk", split_axis=0, concat_axis=0, tiled=True)
    fetched = replies[block_owner, position]
    pieces = []
    for slot_index in range(2 * HALF + 1):
        occupied, virtual = green_pair(fetched[slot_index * per_slot : (slot_index + 1) * per_slot])
        image = image_of(occupied, virtual, source_t)
        pieces.append(pair_block(partners[slot_index], image))
    chi_time = jnp.concatenate(pieces, axis=1)
    column_weights = fold_weights[:, 0]
    weighted = column_weights[:, None, None] * chi_time[None]
    received = lax.all_to_all(weighted, "tau", split_axis=0, concat_axis=0, tiled=True)
    return jnp.sum(received, axis=0, keepdims=True)


def solution(mesh):
    return jax.shard_map(
        local,
        mesh=mesh,
        in_specs=(
            P("blk", None, None, None),
            P("tau", "blk", None),
            P("blk"),
            P("blk"),
            P(None, "tau"),
        ),
        out_specs=P("tau", "blk", None),
        check_vma=False,
    )
```

```python
import jax
import jax.numpy as jnp
from jax import lax
from jax.sharding import PartitionSpec as P


AB = 32
NS = 4
HALF = 1


def from_behind(value, axis, by):
    size = lax.axis_size(axis)
    return lax.ppermute(value, axis, [(i, (i + by) % size) for i in range(size)])


def green_pair(blocks):
    blocks = blocks.reshape(NS, NS, 2, AB, AB)
    occupied = blocks[:, :, 0].transpose(0, 2, 1, 3).reshape(NS * AB, NS * AB)
    virtual = blocks[:, :, 1].transpose(0, 2, 1, 3).reshape(NS * AB, NS * AB)
    return (occupied, virtual)


def image_of(occupied, virtual, source_t):
    halfway = lax.dot_general(
        source_t, virtual, (((2,), (1,)), ((), ())), preferred_element_type=jnp.float32
    ).astype(jnp.bfloat16)
    image = lax.dot_general(
        halfway, occupied, (((1,), (1,)), ((), ())), preferred_element_type=jnp.float32
    ).astype(jnp.bfloat16)
    return image


def pair_block(partner_t, image):
    aux_width = image.shape[0]
    flat_image = image.reshape(aux_width, -1)
    flat_partner = partner_t.reshape(flat_image.shape[1], -1)
    product = jnp.dot(flat_image, flat_partner, preferred_element_type=jnp.float32)
    return -2.0 * product


def partner_from(own_t, by):
    core = lax.axis_index("tau") % 2
    half = own_t.shape[0] // 2
    mine = lax.dynamic_slice_in_dim(own_t, core * half, half, 0)
    fetched = from_behind(mine, "blk", by)
    size = lax.axis_size("tau")
    other = lax.ppermute(fetched, "tau", [(i, i ^ 1) for i in range(size)])
    low = jnp.where(core == 0, fetched, other)
    high = jnp.where(core == 0, other, fetched)
    return jnp.concatenate([low, high], axis=0)


def local_body(three_center, green_blocks, block_owner, block_slot, fold_weights):
    source = three_center[0]
    source_t = jnp.transpose(source, (2, 0, 1))
    own_t = jnp.transpose(source, (1, 0, 2))
    partners = [partner_from(own_t, HALF - j) if j != HALF else own_t for j in range(2 * HALF + 1)]
    local_table = green_blocks[0]
    devices = lax.axis_size("blk")
    requests = block_owner.shape[0]
    per_slot = NS * NS
    capacity = 2 * ((requests + devices - 1) // devices)
    owner_match = (block_owner[:, None] == jnp.arange(devices, dtype=jnp.int32)[None, :]).astype(
        jnp.int32
    )
    position = jnp.sum(jnp.cumsum(owner_match, axis=0) * owner_match, axis=1) - 1
    outgoing = jnp.zeros((devices, capacity), jnp.int32).at[block_owner, position].set(block_slot)
    asked = lax.all_to_all(outgoing, "blk", split_axis=0, concat_axis=0, tiled=True)
    found_blocks = jnp.take(local_table, asked, axis=0)
    replies = lax.all_to_all(found_blocks, "blk", split_axis=0, concat_axis=0, tiled=True)
    fetched = replies[block_owner, position]
    pieces = []
    for slot_index in range(2 * HALF + 1):
        occupied, virtual = green_pair(fetched[slot_index * per_slot : (slot_index + 1) * per_slot])
        image = image_of(occupied, virtual, source_t)
        pieces.append(pair_block(partners[slot_index], image))
    chi_time = jnp.concatenate(pieces, axis=1)
    column_weights = fold_weights[:, 0]
    weighted = column_weights[:, None, None] * chi_time[None]
    received = lax.all_to_all(weighted, "tau", split_axis=0, concat_axis=0, tiled=True)
    return jnp.sum(received, axis=0, keepdims=True)


def solution(mesh):
    return jax.shard_map(
        local_body,
        mesh=mesh,
        in_specs=(
            P("blk", None, None, None),
            P("tau", "blk", None),
            P("blk"),
            P("blk"),
            P(None, "tau"),
        ),
        out_specs=P("tau", "blk", None),
        check_vma=False,
    )
```

```python
import jax
import jax.numpy as jnp
from jax import lax
from jax.sharding import PartitionSpec as P


AB = 32
NS = 4
HALF = 1


def from_behind(value, axis, by):
    size = lax.axis_size(axis)
    return lax.ppermute(value, axis, [(i, (i + by) % size) for i in range(size)])


def green_pair(blocks):
    blocks = blocks.reshape(NS, NS, 2, AB, AB)
    occupied = blocks[:, :, 0].transpose(0, 2, 1, 3).reshape(NS * AB, NS * AB)
    virtual = blocks[:, :, 1].transpose(0, 2, 1, 3).reshape(NS * AB, NS * AB)
    return (occupied, virtual)


def image_of(occupied, virtual, source_t):
    halfway = lax.dot_general(
        source_t, virtual, (((2,), (1,)), ((), ())), preferred_element_type=jnp.float32
    ).astype(jnp.bfloat16)
    image = lax.dot_general(
        halfway, occupied, (((1,), (1,)), ((), ())), preferred_element_type=jnp.float32
    ).astype(jnp.bfloat16)
    return image


def pair_block(partner_t, image):
    aux_width = image.shape[0]
    flat_image = image.reshape(aux_width, -1)
    flat_partner = partner_t.reshape(flat_image.shape[1], -1)
    return jnp.dot(flat_image, flat_partner, preferred_element_type=jnp.float32)


def split_pair_block(halves, image):
    core = lax.axis_index("tau") % 2
    half = image.shape[1] // 2
    mine = lax.dynamic_slice_in_dim(image, core * half, half, 1)
    theirs = lax.dynamic_slice_in_dim(image, (1 - core) * half, half, 1)
    return pair_block(halves[0], mine) + pair_block(halves[1], theirs)


def partner_from(own_t, by, chunks=2):
    core = lax.axis_index("tau") % 2
    half = own_t.shape[0] // 2
    step = half // chunks
    size = lax.axis_size("tau")
    fetched, other = [], []
    for k in range(chunks):
        mine = lax.dynamic_slice_in_dim(own_t, core * half + k * step, step, 0)
        got = from_behind(mine, "blk", by)
        fetched.append(got)
        other.append(lax.ppermute(got, "tau", [(i, i ^ 1) for i in range(size)]))
    return jnp.concatenate(fetched, axis=0), jnp.concatenate(other, axis=0)


def local_body(three_center, green_blocks, block_owner, block_slot, fold_weights):
    source = three_center[0]
    source_t = jnp.transpose(source, (2, 0, 1))
    own_t = jnp.transpose(source, (1, 0, 2))
    partners = [partner_from(own_t, HALF - j) if j != HALF else own_t for j in range(2 * HALF + 1)]
    local_table = green_blocks[0]
    devices = lax.axis_size("blk")
    requests = block_owner.shape[0]
    per_slot = NS * NS
    capacity = 2 * ((requests + devices - 1) // devices)
    owner_match = (block_owner[:, None] == jnp.arange(devices, dtype=jnp.int32)[None, :]).astype(
        jnp.int32
    )
    position = jnp.sum(jnp.cumsum(owner_match, axis=0) * owner_match, axis=1) - 1
    outgoing = jnp.zeros((devices, capacity), jnp.int32).at[block_owner, position].set(block_slot)
    asked = lax.all_to_all(outgoing, "blk", split_axis=0, concat_axis=0, tiled=True)
    found_blocks = jnp.take(local_table, asked, axis=0)
    replies = lax.all_to_all(found_blocks, "blk", split_axis=0, concat_axis=0, tiled=True)
    fetched = replies[block_owner, position]
    pieces = []
    for slot_index in range(2 * HALF + 1):
        occupied, virtual = green_pair(fetched[slot_index * per_slot : (slot_index + 1) * per_slot])
        image = image_of(occupied, virtual, source_t)
        if slot_index == HALF:
            pieces.append(-2.0 * pair_block(partners[slot_index], image))
        else:
            pieces.append(-2.0 * split_pair_block(partners[slot_index], image))
    chi_time = jnp.concatenate(pieces, axis=1)
    column_weights = fold_weights[:, 0]
    weighted = column_weights[:, None, None] * chi_time[None]
    received = lax.all_to_all(weighted, "tau", split_axis=0, concat_axis=0, tiled=True)
    return jnp.sum(received, axis=0, keepdims=True)


def solution(mesh):
    return jax.shard_map(
        local_body,
        mesh=mesh,
        in_specs=(
            P("blk", None, None, None),
            P("tau", "blk", None),
            P("blk"),
            P("blk"),
            P(None, "tau"),
        ),
        out_specs=P("tau", "blk", None),
        check_vma=False,
    )
```

```python
import jax
import jax.numpy as jnp
from jax import lax
from jax.sharding import PartitionSpec as P


AB = 32
NS = 4
HALF = 1


def from_behind(value, axis, by):
    size = lax.axis_size(axis)
    return lax.ppermute(value, axis, [(i, (i + by) % size) for i in range(size)])


def green_pair(blocks):
    blocks = blocks.reshape(NS, NS, 2, AB, AB)
    occupied = blocks[:, :, 0].transpose(0, 2, 1, 3).reshape(NS * AB, NS * AB)
    virtual = blocks[:, :, 1].transpose(0, 2, 1, 3).reshape(NS * AB, NS * AB)
    return (occupied, virtual)


def image_of(occupied, virtual, source_t):
    halfway = lax.dot_general(
        source_t, virtual, (((2,), (1,)), ((), ())), preferred_element_type=jnp.float32
    ).astype(jnp.bfloat16)
    image = lax.dot_general(
        halfway, occupied, (((1,), (1,)), ((), ())), preferred_element_type=jnp.float32
    ).astype(jnp.bfloat16)
    return image


def pair_block(partner_t, image):
    aux_width = image.shape[0]
    flat_image = image.reshape(aux_width, -1)
    flat_partner = partner_t.reshape(flat_image.shape[1], -1)
    return jnp.dot(flat_image, flat_partner, preferred_element_type=jnp.float32)


def split_pair_block(halves, image):
    half = image.shape[1] // 2
    return pair_block(halves[0], image[:, :half]) + pair_block(halves[1], image[:, half:])


def rotate_rows(virtual):
    core = lax.axis_index("tau") % 2
    half = virtual.shape[0] // 2
    doubled = jnp.concatenate([virtual, virtual], axis=0)
    return lax.dynamic_slice_in_dim(doubled, core * half, virtual.shape[0], 0)


def partner_from(own_t, by, chunks=1):
    core = lax.axis_index("tau") % 2
    half = own_t.shape[0] // 2
    step = half // chunks
    size = lax.axis_size("tau")
    fetched, other = [], []
    for k in range(chunks):
        mine = lax.dynamic_slice_in_dim(own_t, core * half + k * step, step, 0)
        got = from_behind(mine, "blk", by)
        fetched.append(got)
        other.append(lax.ppermute(got, "tau", [(i, i ^ 1) for i in range(size)]))
    return jnp.concatenate(fetched, axis=0), jnp.concatenate(other, axis=0)


def local_body(three_center, green_blocks, block_owner, block_slot, fold_weights):
    source = three_center[0]
    source_t = jnp.transpose(source, (2, 0, 1))
    own_t = jnp.transpose(source, (1, 0, 2))
    partners = [partner_from(own_t, HALF - j) if j != HALF else own_t for j in range(2 * HALF + 1)]
    local_table = green_blocks[0]
    devices = lax.axis_size("blk")
    requests = block_owner.shape[0]
    per_slot = NS * NS
    capacity = 2 * ((requests + devices - 1) // devices)
    owner_match = (block_owner[:, None] == jnp.arange(devices, dtype=jnp.int32)[None, :]).astype(
        jnp.int32
    )
    position = jnp.sum(jnp.cumsum(owner_match, axis=0) * owner_match, axis=1) - 1
    place_match = (position[:, None] == jnp.arange(capacity, dtype=jnp.int32)[None, :]).astype(jnp.int32)
    outgoing = jnp.sum(
        owner_match[:, :, None] * place_match[:, None, :] * block_slot[:, None, None], axis=0
    )
    asked = lax.all_to_all(outgoing, "blk", split_axis=0, concat_axis=0, tiled=True)
    found_blocks = jnp.take(local_table, asked, axis=0)
    replies = lax.all_to_all(found_blocks, "blk", split_axis=0, concat_axis=0, tiled=True)
    fetched = replies[block_owner, position]
    pieces = []
    for slot_index in range(2 * HALF + 1):
        occupied, virtual = green_pair(fetched[slot_index * per_slot : (slot_index + 1) * per_slot])
        if slot_index != HALF:
            virtual = rotate_rows(virtual)
        image = image_of(occupied, virtual, source_t)
        if slot_index == HALF:
            pieces.append(-2.0 * pair_block(partners[slot_index], image))
        else:
            pieces.append(-2.0 * split_pair_block(partners[slot_index], image))
    chi_time = jnp.concatenate(pieces, axis=1)
    column_weights = fold_weights[:, 0]
    weighted = column_weights[:, None, None] * chi_time[None]
    received = lax.all_to_all(weighted, "tau", split_axis=0, concat_axis=0, tiled=True)
    return jnp.sum(received, axis=0, keepdims=True)


def solution(mesh):
    return jax.shard_map(
        local_body,
        mesh=mesh,
        in_specs=(
            P("blk", None, None, None),
            P("tau", "blk", None),
            P("blk"),
            P("blk"),
            P(None, "tau"),
        ),
        out_specs=P("tau", "blk", None),
        check_vma=False,
    )
```

```python
import jax
import jax.numpy as jnp
from jax import lax
from jax.sharding import PartitionSpec as P


AB = 32
NS = 4
HALF = 1


def from_behind(value, axis, by):
    size = lax.axis_size(axis)
    return lax.ppermute(value, axis, [(i, (i + by) % size) for i in range(size)])


def green_pair(blocks):
    blocks = blocks.reshape(NS, NS, 2, AB, AB)
    occupied = blocks[:, :, 0].transpose(0, 2, 1, 3).reshape(NS * AB, NS * AB)
    virtual = blocks[:, :, 1].transpose(0, 2, 1, 3).reshape(NS * AB, NS * AB)
    return (occupied, virtual)


def image_of(occupied, virtual, source_t):
    halfway = lax.dot_general(
        source_t, virtual, (((2,), (1,)), ((), ())), preferred_element_type=jnp.float32
    ).astype(jnp.bfloat16)
    image = lax.dot_general(
        halfway, occupied, (((1,), (1,)), ((), ())), preferred_element_type=jnp.float32
    ).astype(jnp.bfloat16)
    return image


def pair_block(partner_t, image):
    aux_width = image.shape[0]
    flat_image = image.reshape(aux_width, -1)
    flat_partner = partner_t.reshape(flat_image.shape[1], -1)
    return jnp.dot(flat_image, flat_partner, preferred_element_type=jnp.float32)


def split_pair_block(halves, image):
    core = lax.axis_index("tau") % 2
    half = image.shape[1] // 2
    mine = lax.dynamic_slice_in_dim(image, core * half, half, 1)
    theirs = lax.dynamic_slice_in_dim(image, (1 - core) * half, half, 1)
    return pair_block(halves[0], mine) + pair_block(halves[1], theirs)


def partner_from(own_t, by, chunks=2):
    core = lax.axis_index("tau") % 2
    half = own_t.shape[0] // 2
    step = half // chunks
    size = lax.axis_size("tau")
    fetched, other = [], []
    for k in range(chunks):
        mine = lax.dynamic_slice_in_dim(own_t, core * half + k * step, step, 0)
        got = from_behind(mine, "blk", by)
        fetched.append(got)
        other.append(lax.ppermute(got, "tau", [(i, i ^ 1) for i in range(size)]))
    return jnp.concatenate(fetched, axis=0), jnp.concatenate(other, axis=0)


def local_body(three_center, green_blocks, block_owner, block_slot, fold_weights):
    source = three_center[0]
    source_t = jnp.transpose(source, (2, 0, 1))
    own_t = jnp.transpose(source, (1, 0, 2))
    partners = [partner_from(own_t, HALF - j) if j != HALF else own_t for j in range(2 * HALF + 1)]
    local_table = green_blocks[0]
    devices = lax.axis_size("blk")
    requests = block_owner.shape[0]
    per_slot = NS * NS
    capacity = 2 * ((requests + devices - 1) // devices)
    owner_match = (block_owner[:, None] == jnp.arange(devices, dtype=jnp.int32)[None, :]).astype(
        jnp.int32
    )
    position = jnp.sum(jnp.cumsum(owner_match, axis=0) * owner_match, axis=1) - 1
    place_match = (position[:, None] == jnp.arange(capacity, dtype=jnp.int32)[None, :]).astype(jnp.int32)
    outgoing = jnp.sum(
        owner_match[:, :, None] * place_match[:, None, :] * block_slot[:, None, None], axis=0
    )
    asked = lax.all_to_all(outgoing, "blk", split_axis=0, concat_axis=0, tiled=True)
    found_blocks = jnp.take(local_table, asked, axis=0)
    replies = lax.all_to_all(found_blocks, "blk", split_axis=0, concat_axis=0, tiled=True)
    fetched = replies[block_owner, position]
    pieces = []
    for slot_index in range(2 * HALF + 1):
        occupied, virtual = green_pair(fetched[slot_index * per_slot : (slot_index + 1) * per_slot])
        image = image_of(occupied, virtual, source_t)
        if slot_index == HALF:
            pieces.append(-2.0 * pair_block(partners[slot_index], image))
        else:
            pieces.append(-2.0 * split_pair_block(partners[slot_index], image))
    column_weights = fold_weights[:, 0][:, None, None]

    def fold(chi):
        received = lax.all_to_all(column_weights * chi[None], "tau", split_axis=0, concat_axis=0, tiled=True)
        return jnp.sum(received, axis=0, keepdims=True)

    own = fold(pieces[HALF])
    sides = fold(jnp.concatenate([pieces[0], pieces[2]], axis=1))
    width = pieces[HALF].shape[1]
    return jnp.concatenate([sides[..., :width], own, sides[..., width:]], axis=2)


def solution(mesh):
    return jax.shard_map(
        local_body,
        mesh=mesh,
        in_specs=(
            P("blk", None, None, None),
            P("tau", "blk", None),
            P("blk"),
            P("blk"),
            P(None, "tau"),
        ),
        out_specs=P("tau", "blk", None),
        check_vma=False,
    )
```

```python
import jax
import jax.numpy as jnp
from jax import lax
from jax.sharding import PartitionSpec as P


AB = 32
NS = 4
HALF = 1


def from_behind(value, axis, by):
    size = lax.axis_size(axis)
    return lax.ppermute(value, axis, [(i, (i + by) % size) for i in range(size)])


def green_pair(blocks):
    blocks = blocks.reshape(NS, NS, 2, AB, AB)
    occupied = blocks[:, :, 0].transpose(0, 2, 1, 3).reshape(NS * AB, NS * AB)
    virtual = blocks[:, :, 1].transpose(0, 2, 1, 3).reshape(NS * AB, NS * AB)
    return (occupied, virtual)


def image_of(occupied, virtual, source_t):
    halfway = lax.dot_general(
        source_t, virtual, (((2,), (1,)), ((), ())), preferred_element_type=jnp.float32
    ).astype(jnp.bfloat16)
    image = lax.dot_general(
        halfway, occupied, (((1,), (1,)), ((), ())), preferred_element_type=jnp.float32
    ).astype(jnp.bfloat16)
    return image


def pair_block(partner_t, image):
    aux_width = image.shape[0]
    flat_image = image.reshape(aux_width, -1)
    flat_partner = partner_t.reshape(flat_image.shape[1], -1)
    return jnp.dot(flat_image, flat_partner, preferred_element_type=jnp.float32)


def split_pair_block(halves, image):
    core = lax.axis_index("tau") % 2
    half = image.shape[1] // 2
    mine = lax.dynamic_slice_in_dim(image, core * half, half, 1)
    theirs = lax.dynamic_slice_in_dim(image, (1 - core) * half, half, 1)
    return pair_block(halves[0], mine) + pair_block(halves[1], theirs)


def partner_from(own_t, by, chunks=2):
    core = lax.axis_index("tau") % 2
    half = own_t.shape[0] // 2
    step = half // chunks
    size = lax.axis_size("tau")
    fetched, other = [], []
    for k in range(chunks):
        mine = lax.dynamic_slice_in_dim(own_t, core * half + k * step, step, 0)
        got = from_behind(mine, "blk", by)
        fetched.append(got)
        other.append(lax.ppermute(got, "tau", [(i, i ^ 1) for i in range(size)]))
    return jnp.concatenate(fetched, axis=0), jnp.concatenate(other, axis=0)


def local_body(three_center, green_blocks, block_owner, block_slot, fold_weights):
    source = three_center[0]
    source_t = jnp.transpose(source, (2, 0, 1))
    own_t = jnp.transpose(source, (1, 0, 2))
    partners = [partner_from(own_t, HALF - j) if j != HALF else own_t for j in range(2 * HALF + 1)]
    local_table = green_blocks[0]
    devices = lax.axis_size("blk")
    requests = block_owner.shape[0]
    per_slot = NS * NS
    capacity = 2 * ((requests + devices - 1) // devices)
    owner_match = (block_owner[:, None] == jnp.arange(devices, dtype=jnp.int32)[None, :]).astype(
        jnp.int32
    )
    position = jnp.sum(jnp.cumsum(owner_match, axis=0) * owner_match, axis=1) - 1
    place_match = (position[:, None] == jnp.arange(capacity, dtype=jnp.int32)[None, :]).astype(jnp.int32)
    outgoing = jnp.sum(
        owner_match[:, :, None] * place_match[:, None, :] * block_slot[:, None, None], axis=0
    )
    asked = lax.all_to_all(outgoing, "blk", split_axis=0, concat_axis=0, tiled=True)
    found_blocks = jnp.take(local_table, asked, axis=0)
    replies = lax.all_to_all(found_blocks, "blk", split_axis=0, concat_axis=0, tiled=True)
    fetched = replies[block_owner, position]
    pieces = []
    for slot_index in range(2 * HALF + 1):
        occupied, virtual = green_pair(fetched[slot_index * per_slot : (slot_index + 1) * per_slot])
        image = image_of(occupied, virtual, source_t)
        if slot_index == HALF:
            half = image.shape[1] // 2
            own_part = pair_block(own_t[:half], image[:, :half]) + pair_block(own_t[half:], image[:, half:])
            pieces.append(-2.0 * own_part)
        else:
            pieces.append(-2.0 * split_pair_block(partners[slot_index], image))
    chi_time = jnp.concatenate(pieces, axis=1)
    column_weights = fold_weights[:, 0]
    weighted = column_weights[:, None, None] * chi_time[None]
    received = lax.all_to_all(weighted, "tau", split_axis=0, concat_axis=0, tiled=True)
    return jnp.sum(received, axis=0, keepdims=True)


def solution(mesh):
    return jax.shard_map(
        local_body,
        mesh=mesh,
        in_specs=(
            P("blk", None, None, None),
            P("tau", "blk", None),
            P("blk"),
            P("blk"),
            P(None, "tau"),
        ),
        out_specs=P("tau", "blk", None),
        check_vma=False,
    )
```

```python
import jax
import jax.numpy as jnp
from jax import lax
from jax.sharding import PartitionSpec as P


AB = 32
NS = 4
HALF = 1


def from_behind(value, axis, by):
    size = lax.axis_size(axis)
    return lax.ppermute(value, axis, [(i, (i + by) % size) for i in range(size)])


def green_pair(blocks):
    blocks = blocks.reshape(NS, NS, 2, AB, AB)
    occupied = blocks[:, :, 0].transpose(0, 2, 1, 3).reshape(NS * AB, NS * AB)
    virtual = blocks[:, :, 1].transpose(0, 2, 1, 3).reshape(NS * AB, NS * AB)
    return (occupied, virtual)


def image_of(occupied, virtual, source_t):
    halfway = lax.dot_general(
        source_t, virtual, (((2,), (1,)), ((), ())), preferred_element_type=jnp.float32
    ).astype(jnp.bfloat16)
    image = lax.dot_general(
        halfway, occupied, (((1,), (1,)), ((), ())), preferred_element_type=jnp.float32
    ).astype(jnp.bfloat16)
    return image


def pair_block(partner_t, image):
    aux_width = image.shape[0]
    flat_image = image.reshape(aux_width, -1)
    flat_partner = partner_t.reshape(flat_image.shape[1], -1)
    return jnp.dot(flat_image, flat_partner, preferred_element_type=jnp.float32)


def split_pair_block(halves, image):
    core = lax.axis_index("tau") % 2
    half = image.shape[1] // 2
    mine = lax.dynamic_slice_in_dim(image, core * half, half, 1)
    theirs = lax.dynamic_slice_in_dim(image, (1 - core) * half, half, 1)
    return pair_block(halves[0], mine) + pair_block(halves[1], theirs)


def partners_from(own_t, chunks=2):
    core = lax.axis_index("tau") % 2
    half = own_t.shape[0] // 2
    step = half // chunks
    size = lax.axis_size("tau")
    fetched, other = {-1: [], 1: []}, {-1: [], 1: []}
    for k in range(chunks):
        mine = lax.dynamic_slice_in_dim(own_t, core * half + k * step, step, 0)
        got = {}
        for by in (1, -1):
            got[by] = from_behind(mine, "blk", by)
        swapped = lax.ppermute(jnp.stack([got[1], got[-1]]), "tau", [(i, i ^ 1) for i in range(size)])
        for n, by in enumerate((1, -1)):
            fetched[by].append(got[by])
            other[by].append(swapped[n])
    return {
        by: (jnp.concatenate(fetched[by], axis=0), jnp.concatenate(other[by], axis=0)) for by in (1, -1)
    }


def local_body(three_center, green_blocks, block_owner, block_slot, fold_weights):
    source = three_center[0]
    source_t = jnp.transpose(source, (2, 0, 1))
    own_t = jnp.transpose(source, (1, 0, 2))
    neighbours = partners_from(own_t)
    partners = [neighbours[HALF - j] if j != HALF else own_t for j in range(2 * HALF + 1)]
    local_table = green_blocks[0]
    devices = lax.axis_size("blk")
    requests = block_owner.shape[0]
    per_slot = NS * NS
    capacity = 2 * ((requests + devices - 1) // devices)
    owner_match = (block_owner[:, None] == jnp.arange(devices, dtype=jnp.int32)[None, :]).astype(
        jnp.int32
    )
    position = jnp.sum(jnp.cumsum(owner_match, axis=0) * owner_match, axis=1) - 1
    place_match = (position[:, None] == jnp.arange(capacity, dtype=jnp.int32)[None, :]).astype(jnp.int32)
    outgoing = jnp.sum(
        owner_match[:, :, None] * place_match[:, None, :] * block_slot[:, None, None], axis=0
    )
    asked = lax.all_to_all(outgoing, "blk", split_axis=0, concat_axis=0, tiled=True)
    found_blocks = jnp.take(local_table, asked, axis=0)
    replies = lax.all_to_all(found_blocks, "blk", split_axis=0, concat_axis=0, tiled=True)
    fetched = replies[block_owner, position]
    pieces = []
    for slot_index in range(2 * HALF + 1):
        occupied, virtual = green_pair(fetched[slot_index * per_slot : (slot_index + 1) * per_slot])
        image = image_of(occupied, virtual, source_t)
        if slot_index == HALF:
            pieces.append(-2.0 * pair_block(partners[slot_index], image))
        else:
            pieces.append(-2.0 * split_pair_block(partners[slot_index], image))
    chi_time = jnp.concatenate(pieces, axis=1)
    column_weights = fold_weights[:, 0]
    weighted = column_weights[:, None, None] * chi_time[None]
    received = lax.all_to_all(weighted, "tau", split_axis=0, concat_axis=0, tiled=True)
    return jnp.sum(received, axis=0, keepdims=True)


def solution(mesh):
    return jax.shard_map(
        local_body,
        mesh=mesh,
        in_specs=(
            P("blk", None, None, None),
            P("tau", "blk", None),
            P("blk"),
            P("blk"),
            P(None, "tau"),
        ),
        out_specs=P("tau", "blk", None),
        check_vma=False,
    )
```

```python
import jax
import jax.numpy as jnp
from jax import lax
from jax.sharding import PartitionSpec as P


AB = 32
NS = 4
HALF = 1


def from_behind(value, axis, by):
    size = lax.axis_size(axis)
    return lax.ppermute(value, axis, [(i, (i + by) % size) for i in range(size)])


def green_pair(blocks):
    blocks = blocks.reshape(NS, NS, 2, AB, AB)
    occupied = blocks[:, :, 0].transpose(0, 2, 1, 3).reshape(NS * AB, NS * AB)
    virtual = blocks[:, :, 1].transpose(0, 2, 1, 3).reshape(NS * AB, NS * AB)
    return (occupied, virtual)


def image_of(occupied, virtual, source_t):
    halfway = lax.dot_general(
        source_t, virtual, (((2,), (1,)), ((), ())), preferred_element_type=jnp.float32
    ).astype(jnp.bfloat16)
    image = lax.dot_general(
        halfway, occupied, (((1,), (1,)), ((), ())), preferred_element_type=jnp.float32
    ).astype(jnp.bfloat16)
    return image


def pair_block(partner_t, image):
    aux_width = image.shape[0]
    flat_image = image.reshape(aux_width, -1)
    flat_partner = partner_t.reshape(flat_image.shape[1], -1)
    return jnp.dot(flat_image, flat_partner, preferred_element_type=jnp.float32)


def split_pair_block(halves, image):
    core = lax.axis_index("tau") % 2
    half = image.shape[1] // 2
    mine = lax.dynamic_slice_in_dim(image, core * half, half, 1)
    theirs = lax.dynamic_slice_in_dim(image, (1 - core) * half, half, 1)
    return pair_block(halves[0], mine) + pair_block(halves[1], theirs)


def partner_from(own_t, by, chunks=2):
    core = lax.axis_index("tau") % 2
    half = own_t.shape[0] // 2
    step = half // chunks
    size = lax.axis_size("tau")
    fetched, other = [], []
    for k in range(chunks):
        mine = lax.dynamic_slice_in_dim(own_t, core * half + k * step, step, 0)
        got = from_behind(mine, "blk", by)
        fetched.append(got)
        other.append(lax.ppermute(got, "tau", [(i, i ^ 1) for i in range(size)]))
    return jnp.concatenate(fetched, axis=0), jnp.concatenate(other, axis=0)


def local_body(three_center, green_blocks, block_owner, block_slot, fold_weights):
    source = three_center[0]
    source_t = jnp.transpose(source, (2, 0, 1))
    own_t = jnp.transpose(source, (1, 0, 2))
    partners = [partner_from(own_t, HALF - j) if j != HALF else own_t for j in range(2 * HALF + 1)]
    local_table = green_blocks[0]
    devices = lax.axis_size("blk")
    requests = block_owner.shape[0]
    per_slot = NS * NS
    capacity = 2 * ((requests + devices - 1) // devices)
    owner_match = (block_owner[:, None] == jnp.arange(devices, dtype=jnp.int32)[None, :]).astype(
        jnp.int32
    )
    position = jnp.sum(jnp.cumsum(owner_match, axis=0) * owner_match, axis=1) - 1
    place_match = (position[:, None] == jnp.arange(capacity, dtype=jnp.int32)[None, :]).astype(jnp.int32)
    outgoing = jnp.sum(
        owner_match[:, :, None] * place_match[:, None, :] * block_slot[:, None, None], axis=0
    )
    asked = lax.all_to_all(outgoing, "blk", split_axis=0, concat_axis=0, tiled=True)
    found_blocks = jnp.take(local_table, asked, axis=0, mode="clip")
    replies = lax.all_to_all(found_blocks, "blk", split_axis=0, concat_axis=0, tiled=True)
    fetched = replies[block_owner, position]
    pieces = []
    for slot_index in range(2 * HALF + 1):
        occupied, virtual = green_pair(fetched[slot_index * per_slot : (slot_index + 1) * per_slot])
        image = image_of(occupied, virtual, source_t)
        if slot_index == HALF:
            pieces.append(-2.0 * pair_block(partners[slot_index], image))
        else:
            pieces.append(-2.0 * split_pair_block(partners[slot_index], image))
    chi_time = jnp.concatenate(pieces, axis=1)
    column_weights = fold_weights[:, 0]
    weighted = column_weights[:, None, None] * chi_time[None]
    received = lax.all_to_all(weighted, "tau", split_axis=0, concat_axis=0, tiled=True)
    return jnp.sum(received, axis=0, keepdims=True)


def solution(mesh):
    return jax.shard_map(
        local_body,
        mesh=mesh,
        in_specs=(
            P("blk", None, None, None),
            P("tau", "blk", None),
            P("blk"),
            P("blk"),
            P(None, "tau"),
        ),
        out_specs=P("tau", "blk", None),
        check_vma=False,
    )
```
